512 devices in a mesh: gx: 32 (over x, y), gy: 16 (over z, core).
Axes of the slice: x: 4, y: 8, z: 8, core: 2. Of those that a mesh axis runs over, the one named last changes fastest.
Arguments:
- test_block: float32 [32, 8, 512, 2048], P(None, None, 'gx', 'gy'), may hold values from -1500 to 1500, as said below
- kappa_sq: float32 [8, 512, 2048], P(None, 'gx', 'gy'), may hold values from 0.05 to 2
Outputs:
- basis: float32 [32, 8, 512, 2048], P(None, None, 'gx', 'gy')
The draws below stay inside these ranges and needn't reach their ends.
Inputs may be any that keep to these rules, and one draw needn't show every extreme that they name: `test_block`: real-valued entries.
All inputs are finite; a program needn't handle non-finite values.
Results may differ from the reference program's by a relative error of at most 0.0003.
Values sent between devices are 32-bit elements; how exact they have to be, the bound alone decides.
No kernel may reach another device: no remote copies, remote signals or barrier semaphores. Data moves between devices by JAX's collectives and lax.ppermute only.
A program may use at most 64 MiB of HBM per device.

```python
import math
import jax
import jax.numpy as jnp
from jax import lax

COLS = 32
NZ = 8
NX = 512
NY = 2048
CELLS = 8388608


def draw_test_block(key, part):
    key_own = jax.random.fold_in(key, 11)
    key_shared = jax.random.fold_in(key, 23)
    key_scale = jax.random.fold_in(key, 37)
    key_weights = jax.random.fold_in(key, 41)
    x_pos = jnp.arange(NX, dtype=jnp.float32) / NX
    y_pos = jnp.arange(NY, dtype=jnp.float32) / NY
    x_upper = (jnp.arange(NX, dtype=jnp.int32) >= NX // 2)[:, None]
    y_upper = (jnp.arange(NY, dtype=jnp.int32) >= NY // 2)[None, :]
    weights = jnp.clip(jax.random.normal(key_weights, (4, COLS), jnp.float32), -2.5, 2.5)
    first = weights[0][:, None, None, None]
    second = weights[1][:, None, None, None]
    third = weights[2][:, None, None, None]
    fourth = weights[3][:, None, None, None]
    region_weight = jnp.where(x_upper, jnp.where(y_upper, fourth, third), jnp.where(y_upper, second, first))
    cell_scale = jnp.exp(jax.random.uniform(key_scale, (1, NZ, NX, NY), jnp.float32) * math.log(10.0))
    own = jnp.clip(jax.random.normal(key_own, (COLS, NZ, NX, NY), jnp.float32), -6.0, 6.0)
    shared = jnp.clip(jax.random.normal(key_shared, (1, NZ, NX, NY), jnp.float32), -6.0, 6.0)
    mixing = 130.0
    trend = (1.0 + 2.0 * x_pos)[:, None] * (1.0 + 2.0 * y_pos)[None, :]
    return cell_scale * trend * (shared * region_weight + own / mixing)


def shard_levels(own_key, dims, shards, low, top_value):
    level, own = 1.0, jax.random.fold_in(own_key, 6)
    for axis_at, shards_of in shards:
        steps = jnp.exp(jax.random.uniform(jax.random.fold_in(own, axis_at), (shards_of,), jnp.float32, low / len(shards), top_value / len(shards)))
        level = level * jnp.repeat(steps, dims[axis_at] // shards_of).reshape([-1 if axis == axis_at else 1 for axis in range(len(dims))])
    return level


def setup_inputs(seed: int = 0) -> dict:
    arg_keys = jax.random.split(jax.random.key(seed), 3)
    return {
        "test_block": draw_test_block(jax.random.fold_in(arg_keys[2], 71), 0),
        "kappa_sq": jnp.clip(jnp.exp(math.log(2.0) - 3.6888794 * jax.random.uniform(arg_keys[1], (NZ, NX, NY), jnp.float32) ** shard_levels(arg_keys[1], (NZ, NX, NY), ((1, 32), (2, 16)), -0.2, 0.2)), 0.05, 2.0),
    }


def stencil(field_in, coefficient):
    padded = jnp.pad(field_in, 1)
    neighbours = padded[1:-1, 2:, 1:-1] + padded[1:-1, :-2, 1:-1]
    neighbours = neighbours + padded[1:-1, 1:-1, 2:] + padded[1:-1, 1:-1, :-2]
    neighbours = neighbours + padded[2:, 1:-1, 1:-1] + padded[:-2, 1:-1, 1:-1]
    return (6.0 + coefficient) * field_in - neighbours

def lower_solve(factor, block):
    return lax.linalg.triangular_solve(factor, block, left_side=True, lower=True)

def reference(test_block, kappa_sq):

    def twice_applied(column):
        return stencil(stencil(column, kappa_sq), kappa_sq)
    sample = lax.map(twice_applied, test_block)
    flattened = sample.reshape(COLS, -1)
    gram_one = jnp.dot(flattened, flattened.T, precision=lax.Precision.HIGHEST)
    factor_one = jnp.linalg.cholesky(gram_one)
    levels = jnp.arange(NZ, dtype=jnp.int32)

    def slab_gram(level):
        slab_block = lax.dynamic_index_in_dim(sample, level, 1, keepdims=False).reshape(COLS, -1)
        partial_value = lower_solve(factor_one, slab_block)
        return jnp.dot(partial_value, partial_value.T, precision=lax.Precision.HIGHEST)
    gram_two = lax.optimization_barrier(jnp.sum(lax.map(slab_gram, levels), axis=0))
    factor_two = jnp.linalg.cholesky(gram_two)
    scale_factor = math.sqrt(CELLS)

    def slab_basis(level):
        slab_block = lax.dynamic_index_in_dim(sample, level, 1, keepdims=False).reshape(COLS, -1)
        partial_value = lower_solve(factor_one, slab_block)
        return lower_solve(factor_two, partial_value) * scale_factor
    stacked = lax.map(slab_basis, levels)
    return stacked.reshape(NZ, COLS, NX, NY).transpose(1, 0, 2, 3)
```

```python
import math

import jax
import jax.numpy as jnp
from jax import lax
from jax.sharding import PartitionSpec as P

HIGHEST = lax.Precision.HIGHEST


def shifted_in(lower_part, upper_part, axis):
    count = lax.axis_size(axis)
    forward = [(i, i + 1) for i in range(count - 1)]
    backward = [(i + 1, i) for i in range(count - 1)]
    from_below = lax.ppermute(lower_part, axis, forward)
    from_above = lax.ppermute(upper_part, axis, backward)
    return from_below, from_above


def extend(block, width):
    below, above = shifted_in(block[:, :, -width:, :], block[:, :, :width, :], "gx")
    block = jnp.concatenate([below, block, above], axis=2)
    left, right = shifted_in(block[..., -width:], block[..., :width], "gy")
    return jnp.concatenate([left, block, right], axis=3)


def stencil(padded, coefficient):
    center = padded[:, :, 1:-1, 1:-1]
    neighbours = padded[:, :, 2:, 1:-1] + padded[:, :, :-2, 1:-1]
    neighbours = neighbours + padded[:, :, 1:-1, 2:] + padded[:, :, 1:-1, :-2]
    z_padded = jnp.pad(center, ((0, 0), (1, 1), (0, 0), (0, 0)))
    neighbours = neighbours + z_padded[:, 2:] + z_padded[:, :-2]
    return (6.0 + coefficient) * center - neighbours


def inside_mask(x_cells, y_cells):
    ix, iy = lax.axis_index("gx"), lax.axis_index("gy")
    nx, ny = lax.axis_size("gx"), lax.axis_size("gy")
    rows = lax.broadcasted_iota(jnp.int32, (x_cells + 2, y_cells + 2), 0)
    cols = lax.broadcasted_iota(jnp.int32, (x_cells + 2, y_cells + 2), 1)
    row_ok = ((rows > 0) | (ix > 0)) & ((rows < x_cells + 1) | (ix < nx - 1))
    col_ok = ((cols > 0) | (iy > 0)) & ((cols < y_cells + 1) | (iy < ny - 1))
    return row_ok & col_ok


def butterfly_sum(value):
    for axis in ("gy", "gx"):
        count = lax.axis_size(axis)
        step = 1
        while step < count:
            pairs = [(i, i ^ step) for i in range(count)]
            value = value + lax.ppermute(value, axis, pairs)
            step *= 2
    return value


def gram(block):
    return jnp.einsum("czxy,dzxy->cd", block, block, precision=HIGHEST)


def inverse_factor(gram_matrix):
    factor = jnp.linalg.cholesky(gram_matrix)
    eye = jnp.eye(factor.shape[0], dtype=factor.dtype)
    return lax.linalg.triangular_solve(factor, eye, left_side=True, lower=True)


def body(test_block, kappa_sq):
    cols_here, depth_here, x_cells, y_cells = test_block.shape
    joined = jnp.concatenate([test_block, kappa_sq[None]], axis=0)
    padded = extend(joined, 2)
    field_ext, kappa_ext = padded[:cols_here], padded[cols_here]
    once = stencil(field_ext, kappa_ext[None, :, 1:-1, 1:-1])
    once = jnp.where(inside_mask(x_cells, y_cells), once, 0.0)
    sample = stencil(once, kappa_sq)
    inverse_one = inverse_factor(butterfly_sum(gram(sample)))
    partial_value = jnp.einsum("cd,dzxy->czxy", inverse_one, sample, precision=HIGHEST)
    inverse_two = inverse_factor(butterfly_sum(gram(partial_value)))
    cells = depth_here * x_cells * y_cells * lax.axis_size("gx") * lax.axis_size("gy")
    result = jnp.einsum("cd,dzxy->czxy", inverse_two, partial_value, precision=HIGHEST)
    return result * math.sqrt(cells)


def solution(mesh):
    in_specs = (P(None, None, "gx", "gy"), P(None, "gx", "gy"))
    out_specs = P(None, None, "gx", "gy")
    return jax.shard_map(body, mesh=mesh, in_specs=in_specs, out_specs=out_specs, check_vma=False)
```

```python
import math

import jax
import jax.numpy as jnp
from jax import lax
from jax.sharding import PartitionSpec as P

HIGHEST = lax.Precision.HIGHEST


def shifted_in(lower_part, upper_part, axis):
    count = lax.axis_size(axis)
    forward = [(i, i + 1) for i in range(count - 1)]
    backward = [(i + 1, i) for i in range(count - 1)]
    from_below = lax.ppermute(lower_part, axis, forward)
    from_above = lax.ppermute(upper_part, axis, backward)
    return from_below, from_above


def extend(block, width):
    below, above = shifted_in(block[:, :, -width:, :], block[:, :, :width, :], "gx")
    block = jnp.concatenate([below, block, above], axis=2)
    left, right = shifted_in(block[..., -width:], block[..., :width], "gy")
    return jnp.concatenate([left, block, right], axis=3)


def stencil(padded, coefficient):
    center = padded[:, :, 1:-1, 1:-1]
    neighbours = padded[:, :, 2:, 1:-1] + padded[:, :, :-2, 1:-1]
    neighbours = neighbours + padded[:, :, 1:-1, 2:] + padded[:, :, 1:-1, :-2]
    z_padded = jnp.pad(center, ((0, 0), (1, 1), (0, 0), (0, 0)))
    neighbours = neighbours + z_padded[:, 2:] + z_padded[:, :-2]
    return (6.0 + coefficient) * center - neighbours


def inside_mask(x_cells, y_cells):
    ix, iy = lax.axis_index("gx"), lax.axis_index("gy")
    nx, ny = lax.axis_size("gx"), lax.axis_size("gy")
    rows = lax.broadcasted_iota(jnp.int32, (x_cells + 2, y_cells + 2), 0)
    cols = lax.broadcasted_iota(jnp.int32, (x_cells + 2, y_cells + 2), 1)
    row_ok = ((rows > 0) | (ix > 0)) & ((rows < x_cells + 1) | (ix < nx - 1))
    col_ok = ((cols > 0) | (iy > 0)) & ((cols < y_cells + 1) | (iy < ny - 1))
    return row_ok & col_ok


def butterfly_sum(value):
    value = jnp.sum(lax.all_gather(value, "gy"), axis=0)
    count = lax.axis_size("gx")
    step = 1
    while step < count:
        pairs = [(i, i ^ step) for i in range(count)]
        value = value + lax.ppermute(value, "gx", pairs)
        step *= 2
    return value


def gram(block):
    return jnp.einsum("czxy,dzxy->cd", block, block, precision=HIGHEST)


def inverse_factor(gram_matrix):
    factor = jnp.linalg.cholesky(gram_matrix)
    eye = jnp.eye(factor.shape[0], dtype=factor.dtype)
    return lax.linalg.triangular_solve(factor, eye, left_side=True, lower=True)


def body(test_block, kappa_sq):
    cols_here, depth_here, x_cells, y_cells = test_block.shape
    joined = jnp.concatenate([test_block, kappa_sq[None]], axis=0)
    padded = extend(joined, 2)
    field_ext, kappa_ext = padded[:cols_here], padded[cols_here]
    once = stencil(field_ext, kappa_ext[None, :, 1:-1, 1:-1])
    once = jnp.where(inside_mask(x_cells, y_cells), once, 0.0)
    sample = stencil(once, kappa_sq)
    inverse_one = inverse_factor(butterfly_sum(gram(sample)))
    partial_value = jnp.einsum("cd,dzxy->czxy", inverse_one, sample, precision=HIGHEST)
    inverse_two = inverse_factor(butterfly_sum(gram(partial_value)))
    cells = depth_here * x_cells * y_cells * lax.axis_size("gx") * lax.axis_size("gy")
    result = jnp.einsum("cd,dzxy->czxy", inverse_two, partial_value, precision=HIGHEST)
    return result * math.sqrt(cells)


def solution(mesh):
    in_specs = (P(None, None, "gx", "gy"), P(None, "gx", "gy"))
    out_specs = P(None, None, "gx", "gy")
    return jax.shard_map(body, mesh=mesh, in_specs=in_specs, out_specs=out_specs, check_vma=False)
```

```python
import math

import jax
import jax.numpy as jnp
from jax import lax
from jax.sharding import PartitionSpec as P

HIGHEST = lax.Precision.HIGHEST


def shifted_in(lower_part, upper_part, axis):
    count = lax.axis_size(axis)
    forward = [(i, i + 1) for i in range(count - 1)]
    backward = [(i + 1, i) for i in range(count - 1)]
    from_below = lax.ppermute(lower_part, axis, forward)
    from_above = lax.ppermute(upper_part, axis, backward)
    return from_below, from_above


def extend(block, width):
    below, above = shifted_in(block[:, :, -width:, :], block[:, :, :width, :], "gx")
    block = jnp.concatenate([below, block, above], axis=2)
    left, right = shifted_in(block[..., -width:], block[..., :width], "gy")
    return jnp.concatenate([left, block, right], axis=3)


def stencil(padded, coefficient):
    center = padded[:, :, 1:-1, 1:-1]
    neighbours = padded[:, :, 2:, 1:-1] + padded[:, :, :-2, 1:-1]
    neighbours = neighbours + padded[:, :, 1:-1, 2:] + padded[:, :, 1:-1, :-2]
    z_padded = jnp.pad(center, ((0, 0), (1, 1), (0, 0), (0, 0)))
    neighbours = neighbours + z_padded[:, 2:] + z_padded[:, :-2]
    return (6.0 + coefficient) * center - neighbours


def inside_mask(x_cells, y_cells):
    ix, iy = lax.axis_index("gx"), lax.axis_index("gy")
    nx, ny = lax.axis_size("gx"), lax.axis_size("gy")
    rows = lax.broadcasted_iota(jnp.int32, (x_cells + 2, y_cells + 2), 0)
    cols = lax.broadcasted_iota(jnp.int32, (x_cells + 2, y_cells + 2), 1)
    row_ok = ((rows > 0) | (ix > 0)) & ((rows < x_cells + 1) | (ix < nx - 1))
    col_ok = ((cols > 0) | (iy > 0)) & ((cols < y_cells + 1) | (iy < ny - 1))
    return row_ok & col_ok


def butterfly_sum(value):
    value = jnp.sum(lax.all_gather(value, "gy"), axis=0)
    for partner in gx_partners(lax.axis_size("gx")):
        value = value + lax.ppermute(value, "gx", [(i, partner(i)) for i in range(len(partner.table))])
    return value


class Partner:
    def __init__(self, table):
        self.table = table

    def __call__(self, i):
        return self.table[i]


def gx_partners(count):
    inner = 8 if count % 8 == 0 else count
    rounds = []
    for size, stride in ((inner, 1), (count // inner, inner)):
        group = 2
        while group <= size:
            table = []
            for i in range(count):
                digit = (i // stride) % size
                base = digit - digit % group
                if group == size and size > 2:
                    other = base + (group - 1 - (digit - base))
                else:
                    other = digit ^ (group // 2)
                table.append(i + (other - digit) * stride)
            rounds.append(Partner(table))
            group *= 2
    return rounds


def gram(block):
    return jnp.einsum("czxy,dzxy->cd", block, block, precision=HIGHEST)


def inverse_factor(gram_matrix):
    factor = jnp.linalg.cholesky(gram_matrix)
    eye = jnp.eye(factor.shape[0], dtype=factor.dtype)
    return lax.linalg.triangular_solve(factor, eye, left_side=True, lower=True)


def body(test_block, kappa_sq):
    cols_here, depth_here, x_cells, y_cells = test_block.shape
    joined = jnp.concatenate([test_block, kappa_sq[None]], axis=0)
    padded = extend(joined, 2)
    field_ext, kappa_ext = padded[:cols_here], padded[cols_here]
    once = stencil(field_ext, kappa_ext[None, :, 1:-1, 1:-1])
    once = jnp.where(inside_mask(x_cells, y_cells), once, 0.0)
    sample = stencil(once, kappa_sq)
    inverse_one = inverse_factor(butterfly_sum(gram(sample)))
    partial_value = jnp.einsum("cd,dzxy->czxy", inverse_one, sample, precision=HIGHEST)
    inverse_two = inverse_factor(butterfly_sum(gram(partial_value)))
    cells = depth_here * x_cells * y_cells * lax.axis_size("gx") * lax.axis_size("gy")
    result = jnp.einsum("cd,dzxy->czxy", inverse_two, partial_value, precision=HIGHEST)
    return result * math.sqrt(cells)


def solution(mesh):
    in_specs = (P(None, None, "gx", "gy"), P(None, "gx", "gy"))
    out_specs = P(None, None, "gx", "gy")
    return jax.shard_map(body, mesh=mesh, in_specs=in_specs, out_specs=out_specs, check_vma=False)
```

```python
import math

import jax
import jax.numpy as jnp
from jax import lax
from jax.experimental import pallas as pl
from jax.experimental.pallas import tpu as pltpu
from jax.sharding import PartitionSpec as P

HIGHEST = lax.Precision.HIGHEST


def shifted_in(lower_part, upper_part, axis):
    count = lax.axis_size(axis)
    forward = [(i, i + 1) for i in range(count - 1)]
    backward = [(i + 1, i) for i in range(count - 1)]
    from_below = lax.ppermute(lower_part, axis, forward)
    from_above = lax.ppermute(upper_part, axis, backward)
    return from_below, from_above


def _zs(v, up):
    zero = jnp.zeros_like(v[:1])
    return jnp.concatenate([v[1:], zero], 0) if up else jnp.concatenate([zero, v[:-1]], 0)


def _sten(center, xu, xd, yu, yd, coef):
    nb = xu + xd
    nb = nb + yu + yd
    nb = nb + _zs(center, True) + _zs(center, False)
    return (6.0 + coef) * center - nb


def _kernel(flags, f_ref, k_ref, xl_ref, xh_ref, kxl_ref, kxh_ref, yl_ref, yr_ref, kyl_ref, kyr_ref, o_ref):
    f = f_ref[0]
    k = k_ref[...]
    xl = xl_ref[0]; xh = xh_ref[0]
    kxl = kxl_ref[...]; kxh = kxh_ref[...]
    yl = yl_ref[0]; yr = yr_ref[0]
    kyl = kyl_ref[...]; kyr = kyr_ref[...]
    nz, nx, ny = f.shape
    row = lax.broadcasted_iota(jnp.int32, f.shape, 1)
    lane = lax.broadcasted_iota(jnp.int32, f.shape, 2)
    lane_r = lax.broadcasted_iota(jnp.int32, (nz, 1, ny), 2)

    def xshift(v, top, bot, up):
        if up:
            return jnp.where(row == nx - 1, bot, pltpu.roll(v, nx - 1, 1))
        return jnp.where(row == 0, top, pltpu.roll(v, 1, 1))

    def yshift(v, left, right, up, lanes):
        if up:
            return jnp.where(lanes == ny - 1, right, pltpu.roll(v, ny - 1, 2))
        return jnp.where(lanes == 0, left, pltpu.roll(v, 1, 2))

    ycl, ycr = yl[:, 2:nx + 2, 1:2], yr[:, 2:nx + 2, 0:1]
    main = _sten(f, xshift(f, xl[:, 1:2], xh[:, 0:1], True), xshift(f, xl[:, 1:2], xh[:, 0:1], False),
                 yshift(f, ycl, ycr, True, lane), yshift(f, ycl, ycr, False, lane), k)
    top_c, bot_c = xl[:, 1:2], xh[:, 0:1]
    top = _sten(top_c, f[:, 0:1], xl[:, 0:1],
                yshift(top_c, yl[:, 1:2, 1:2], yr[:, 1:2, 0:1], True, lane_r),
                yshift(top_c, yl[:, 1:2, 1:2], yr[:, 1:2, 0:1], False, lane_r), kxl)
    bot = _sten(bot_c, xh[:, 1:2], f[:, nx - 1:nx],
                yshift(bot_c, yl[:, nx + 2:nx + 3, 1:2], yr[:, nx + 2:nx + 3, 0:1], True, lane_r),
                yshift(bot_c, yl[:, nx + 2:nx + 3, 1:2], yr[:, nx + 2:nx + 3, 0:1], False, lane_r), kxh)
    left = _sten(ycl, yl[:, 3:nx + 3, 1:2], yl[:, 1:nx + 1, 1:2], f[:, :, 0:1], yl[:, 2:nx + 2, 0:1], kyl)
    right = _sten(ycr, yr[:, 3:nx + 3, 0:1], yr[:, 1:nx + 1, 0:1], yr[:, 2:nx + 2, 1:2], f[:, :, ny - 1:ny], kyr)
    top = jnp.where(flags[0] > 0, top, 0.0)
    bot = jnp.where(flags[1] > 0, bot, 0.0)
    left = jnp.where(flags[2] > 0, left, 0.0)
    right = jnp.where(flags[3] > 0, right, 0.0)
    o_ref[0] = _sten(main, xshift(main, top, bot, True), xshift(main, top, bot, False),
                     yshift(main, left, right, True, lane), yshift(main, left, right, False, lane), k)


def twice_kernel(flags, f, k, xl, xh, kxl, kxh, yl, yr, kyl, kyr):
    cols, nz, nx, ny = f.shape
    blk = lambda shape: pl.BlockSpec((1,) + shape, lambda c, fl: (c,) + (0,) * len(shape))
    full = lambda shape: pl.BlockSpec(shape, lambda c, fl: (0,) * len(shape))
    gs = pltpu.PrefetchScalarGridSpec(
        num_scalar_prefetch=1, grid=(cols,),
        in_specs=[blk((nz, nx, ny)), full((nz, nx, ny)), blk((nz, 2, ny)), blk((nz, 2, ny)),
                  full((nz, 1, ny)), full((nz, 1, ny)), blk((nz, nx + 4, 2)), blk((nz, nx + 4, 2)),
                  full((nz, nx, 1)), full((nz, nx, 1))],
        out_specs=blk((nz, nx, ny)))
    return pl.pallas_call(
        _kernel, grid_spec=gs, out_shape=jax.ShapeDtypeStruct(f.shape, f.dtype),
        cost_estimate=pl.CostEstimate(flops=40 * f.size, bytes_accessed=8 * f.size, transcendentals=0),
    )(flags, f, k, xl, xh, kxl, kxh, yl, yr, kyl, kyr)


def butterfly_sum(value):
    value = jnp.sum(lax.all_gather(value, "gy"), axis=0)
    for partner in gx_partners(lax.axis_size("gx")):
        value = value + lax.ppermute(value, "gx", [(i, partner(i)) for i in range(len(partner.table))])
    return value


class Partner:
    def __init__(self, table):
        self.table = table

    def __call__(self, i):
        return self.table[i]


def gx_partners(count):
    inner = 8 if count % 8 == 0 else count
    rounds = []
    for size, stride in ((inner, 1), (count // inner, inner)):
        group = 2
        while group <= size:
            table = []
            for i in range(count):
                digit = (i // stride) % size
                base = digit - digit % group
                if group == size and size > 2:
                    other = base + (group - 1 - (digit - base))
                else:
                    other = digit ^ (group // 2)
                table.append(i + (other - digit) * stride)
            rounds.append(Partner(table))
            group *= 2
    return rounds


def gram(block):
    return jnp.einsum("czxy,dzxy->cd", block, block, precision=HIGHEST)


def inverse_factor(gram_matrix):
    factor = jnp.linalg.cholesky(gram_matrix)
    eye = jnp.eye(factor.shape[0], dtype=factor.dtype)
    return lax.linalg.triangular_solve(factor, eye, left_side=True, lower=True)


def body(test_block, kappa_sq):
    cols_here, depth_here, x_cells, y_cells = test_block.shape
    joined = jnp.concatenate([test_block, kappa_sq[None]], axis=0)
    below, above = shifted_in(joined[:, :, -2:, :], joined[:, :, :2, :], "gx")
    ext = jnp.concatenate([below, joined, above], axis=2)
    left, right = shifted_in(ext[..., -2:], ext[..., :2], "gy")
    ix, iy = lax.axis_index("gx"), lax.axis_index("gy")
    nx, ny = lax.axis_size("gx"), lax.axis_size("gy")
    flags = jnp.stack([ix > 0, ix < nx - 1, iy > 0, iy < ny - 1]).astype(jnp.int32)
    c = cols_here
    sample = twice_kernel(
        flags, test_block, kappa_sq, below[:c], above[:c], below[c][:, 1:2], above[c][:, 0:1],
        left[:c], right[:c], left[c][:, 2:x_cells + 2, 1:2], right[c][:, 2:x_cells + 2, 0:1],
    )
    inverse_one = inverse_factor(butterfly_sum(gram(sample)))
    partial_value = jnp.einsum("cd,dzxy->czxy", inverse_one, sample, precision=HIGHEST)
    inverse_two = inverse_factor(butterfly_sum(gram(partial_value)))
    cells = depth_here * x_cells * y_cells * lax.axis_size("gx") * lax.axis_size("gy")
    result = jnp.einsum("cd,dzxy->czxy", inverse_two, partial_value, precision=HIGHEST)
    return result * math.sqrt(cells)


def solution(mesh):
    in_specs = (P(None, None, "gx", "gy"), P(None, "gx", "gy"))
    out_specs = P(None, None, "gx", "gy")
    return jax.shard_map(body, mesh=mesh, in_specs=in_specs, out_specs=out_specs, check_vma=False)
```

```python
import math

import jax
import jax.numpy as jnp
from jax import lax
from jax.sharding import PartitionSpec as P

HIGHEST = lax.Precision.HIGHEST


def shifted_in(lower_part, upper_part, axis):
    count = lax.axis_size(axis)
    forward = [(i, i + 1) for i in range(count - 1)]
    backward = [(i + 1, i) for i in range(count - 1)]
    from_below = lax.ppermute(lower_part, axis, forward)
    from_above = lax.ppermute(upper_part, axis, backward)
    return from_below, from_above


def extend(block, width):
    below, above = shifted_in(block[:, :, -width:, :], block[:, :, :width, :], "gx")
    block = jnp.concatenate([below, block, above], axis=2)
    left, right = shifted_in(block[..., -width:], block[..., :width], "gy")
    return jnp.concatenate([left, block, right], axis=3)


def stencil(padded, coefficient):
    center = padded[:, :, 1:-1, 1:-1]
    neighbours = padded[:, :, 2:, 1:-1] + padded[:, :, :-2, 1:-1]
    neighbours = neighbours + padded[:, :, 1:-1, 2:] + padded[:, :, 1:-1, :-2]
    z_padded = jnp.pad(center, ((0, 0), (1, 1), (0, 0), (0, 0)))
    neighbours = neighbours + z_padded[:, 2:] + z_padded[:, :-2]
    return (6.0 + coefficient) * center - neighbours


def inside_mask(x_cells, y_cells):
    ix, iy = lax.axis_index("gx"), lax.axis_index("gy")
    nx, ny = lax.axis_size("gx"), lax.axis_size("gy")
    rows = lax.broadcasted_iota(jnp.int32, (x_cells + 2, y_cells + 2), 0)
    cols = lax.broadcasted_iota(jnp.int32, (x_cells + 2, y_cells + 2), 1)
    row_ok = ((rows > 0) | (ix > 0)) & ((rows < x_cells + 1) | (ix < nx - 1))
    col_ok = ((cols > 0) | (iy > 0)) & ((cols < y_cells + 1) | (iy < ny - 1))
    return row_ok & col_ok


def butterfly_sum(value):
    count = lax.axis_size("gy")
    copies = jnp.broadcast_to(value[None], (count,) + value.shape)
    value = jnp.sum(lax.all_to_all(copies, "gy", 0, 0, tiled=True), axis=0)
    for partner in gx_partners(lax.axis_size("gx")):
        value = value + lax.ppermute(value, "gx", [(i, partner(i)) for i in range(len(partner.table))])
    return value


class Partner:
    def __init__(self, table):
        self.table = table

    def __call__(self, i):
        return self.table[i]


def gx_partners(count):
    inner = 8 if count % 8 == 0 else count
    rounds = []
    for size, stride in ((inner, 1), (count // inner, inner)):
        group = 2
        while group <= size:
            table = []
            for i in range(count):
                digit = (i // stride) % size
                base = digit - digit % group
                if group == size and size > 2:
                    other = base + (group - 1 - (digit - base))
                else:
                    other = digit ^ (group // 2)
                table.append(i + (other - digit) * stride)
            rounds.append(Partner(table))
            group *= 2
    return rounds


def gram(block):
    return jnp.einsum("czxy,dzxy->cd", block, block, precision=HIGHEST)


def inverse_factor(gram_matrix):
    factor = jnp.linalg.cholesky(gram_matrix)
    eye = jnp.eye(factor.shape[0], dtype=factor.dtype)
    return lax.linalg.triangular_solve(factor, eye, left_side=True, lower=True)


def body(test_block, kappa_sq):
    cols_here, depth_here, x_cells, y_cells = test_block.shape
    joined = jnp.concatenate([test_block, kappa_sq[None]], axis=0)
    padded = extend(joined, 2)
    field_ext, kappa_ext = padded[:cols_here], padded[cols_here]
    once = stencil(field_ext, kappa_ext[None, :, 1:-1, 1:-1])
    once = jnp.where(inside_mask(x_cells, y_cells), once, 0.0)
    sample = stencil(once, kappa_sq)
    inverse_one = inverse_factor(butterfly_sum(gram(sample)))
    partial_value = jnp.einsum("cd,dzxy->czxy", inverse_one, sample, precision=HIGHEST)
    inverse_two = inverse_factor(butterfly_sum(gram(partial_value)))
    cells = depth_here * x_cells * y_cells * lax.axis_size("gx") * lax.axis_size("gy")
    result = jnp.einsum("cd,dzxy->czxy", inverse_two, partial_value, precision=HIGHEST)
    return result * math.sqrt(cells)


def solution(mesh):
    in_specs = (P(None, None, "gx", "gy"), P(None, "gx", "gy"))
    out_specs = P(None, None, "gx", "gy")
    return jax.shard_map(body, mesh=mesh, in_specs=in_specs, out_specs=out_specs, check_vma=False)
```

```python
import math

import jax
import jax.numpy as jnp
from jax import lax
from jax.sharding import PartitionSpec as P

HIGHEST = lax.Precision.HIGHEST


def shifted_in(lower_part, upper_part, axis):
    count = lax.axis_size(axis)
    forward = [(i, i + 1) for i in range(count - 1)]
    backward = [(i + 1, i) for i in range(count - 1)]
    from_below = lax.ppermute(lower_part, axis, forward)
    from_above = lax.ppermute(upper_part, axis, backward)
    return from_below, from_above


def extend(block, width):
    below, above = shifted_in(block[:, :, -width:, :], block[:, :, :width, :], "gx")
    block = jnp.concatenate([below, block, above], axis=2)
    left, right = shifted_in(block[..., -width:], block[..., :width], "gy")
    return jnp.concatenate([left, block, right], axis=3)


def stencil(padded, coefficient):
    center = padded[:, :, 1:-1, 1:-1]
    neighbours = padded[:, :, 2:, 1:-1] + padded[:, :, :-2, 1:-1]
    neighbours = neighbours + padded[:, :, 1:-1, 2:] + padded[:, :, 1:-1, :-2]
    z_padded = jnp.pad(center, ((0, 0), (1, 1), (0, 0), (0, 0)))
    neighbours = neighbours + z_padded[:, 2:] + z_padded[:, :-2]
    return (6.0 + coefficient) * center - neighbours


def inside_mask(x_cells, y_cells):
    ix, iy = lax.axis_index("gx"), lax.axis_index("gy")
    nx, ny = lax.axis_size("gx"), lax.axis_size("gy")
    rows = lax.broadcasted_iota(jnp.int32, (x_cells + 2, y_cells + 2), 0)
    cols = lax.broadcasted_iota(jnp.int32, (x_cells + 2, y_cells + 2), 1)
    row_ok = ((rows > 0) | (ix > 0)) & ((rows < x_cells + 1) | (ix < nx - 1))
    col_ok = ((cols > 0) | (iy > 0)) & ((cols < y_cells + 1) | (iy < ny - 1))
    return row_ok & col_ok


def butterfly_sum(value):
    for axis in ("gy", "gx"):
        count = lax.axis_size(axis)
        copies = jnp.broadcast_to(value[None], (count,) + value.shape)
        value = jnp.sum(lax.all_to_all(copies, axis, 0, 0, tiled=True), axis=0)
    return value


def gram(block):
    return jnp.einsum("czxy,dzxy->cd", block, block, precision=HIGHEST)


def inverse_factor(gram_matrix):
    factor = jnp.linalg.cholesky(gram_matrix)
    eye = jnp.eye(factor.shape[0], dtype=factor.dtype)
    return lax.linalg.triangular_solve(factor, eye, left_side=True, lower=True)


def body(test_block, kappa_sq):
    cols_here, depth_here, x_cells, y_cells = test_block.shape
    joined = jnp.concatenate([test_block, kappa_sq[None]], axis=0)
    padded = extend(joined, 2)
    field_ext, kappa_ext = padded[:cols_here], padded[cols_here]
    once = stencil(field_ext, kappa_ext[None, :, 1:-1, 1:-1])
    once = jnp.where(inside_mask(x_cells, y_cells), once, 0.0)
    sample = stencil(once, kappa_sq)
    inverse_one = inverse_factor(butterfly_sum(gram(sample)))
    partial_value = jnp.einsum("cd,dzxy->czxy", inverse_one, sample, precision=HIGHEST)
    inverse_two = inverse_factor(butterfly_sum(gram(partial_value)))
    cells = depth_here * x_cells * y_cells * lax.axis_size("gx") * lax.axis_size("gy")
    result = jnp.einsum("cd,dzxy->czxy", inverse_two, partial_value, precision=HIGHEST)
    return result * math.sqrt(cells)


def solution(mesh):
    in_specs = (P(None, None, "gx", "gy"), P(None, "gx", "gy"))
    out_specs = P(None, None, "gx", "gy")
    return jax.shard_map(body, mesh=mesh, in_specs=in_specs, out_specs=out_specs, check_vma=False)
```
